32 devices in a mesh: dp: 2 (over y), seq: 16 (over z, x, core).
Axes of the slice: x: 2, y: 2, z: 4, core: 2. Of those that a mesh axis runs over, the one named last changes fastest.
Arguments:
- inputs: bfloat16 [2, 256, 512, 512], P('dp', 'seq'), may hold values from -6 to 6
- gate_logits: bfloat16 [2, 256, 512, 512], P('dp', 'seq'), may hold values from -8 to 8
- kernel: bfloat16 [256, 512, 512], P(None, 'seq'), may hold values from -1.5 to 1.5
- cotangent: bfloat16 [2, 256, 512, 512], P('dp', 'seq'), may hold values from -6 to 6
- block_one: bfloat16 [256, 512, 512], P('seq'), may hold values from -0.25 to 0.25
- block_two: bfloat16 [512, 256, 256], P('seq'), may hold values from -0.375 to 0.375
Outputs:
- output: bfloat16 [2, 256, 512, 512], P('dp', 'seq')
- grad_inputs: bfloat16 [2, 256, 512, 512], P('dp', 'seq')
- grad_gate: bfloat16 [2, 256, 512, 512], P('dp', 'seq')
- grad_kernel: bfloat16 [256, 512, 512], P(None, 'seq', 'dp')
- grad_block_one: bfloat16 [256, 512, 512], P('seq', None, 'dp')
- grad_block_two: bfloat16 [512, 256, 256], P('seq', None, 'dp')
The draws below stay inside these ranges and needn't reach their ends.
All inputs are finite; a program needn't handle non-finite values.
Results may differ from the reference program's by a relative error of at most 0.009.
Values may be sent and summed in bfloat16 or wider, within the bound.
No kernel may reach another device: no remote copies, remote signals or barrier semaphores. Data moves between devices by JAX's collectives and lax.ppermute only.
A program may use at most 320 MiB of HBM per device.

```python
import jax
import jax.numpy as jnp
from jax import lax

D = 512
BLOCK = 512
NBLK = 256
SEQS = 2


def block_scale(rng, shape, split, smallest, high):
    gain = 1.0
    for axis_at, blocks in split:
        draws = jax.random.uniform(jax.random.fold_in(jax.random.fold_in(rng, 6), axis_at), (blocks,), jnp.float32, smallest / len(split), high / len(split))
        gain = gain * jnp.repeat(jnp.exp(draws), shape[axis_at] // blocks).reshape((-1,) + (1,) * (len(shape) - 1 - axis_at))
    return gain


def scatter_about(own_key, shape, scale, most, shards=(), dtype=jnp.bfloat16):
    factor_of = block_scale(own_key, shape, shards, -0.22, 0.18) if shards else 1.0
    values = jax.random.normal(own_key, shape, jnp.float32) * scale * factor_of
    return jnp.minimum(jnp.maximum(values, -most), most).astype(dtype)


def setup_inputs(seed: int = 0) -> dict:
    key_of = jax.random.split(jax.random.key(seed), 7)
    return {
        "inputs": scatter_about(key_of[0], (SEQS, NBLK, BLOCK, D), 1.0, 6.0, ((0, 2), (1, 16))),
        "gate_logits": scatter_about(key_of[1], (SEQS, NBLK, BLOCK, D), 2.0, 8.0, ((0, 2), (1, 16))),
        "kernel": jnp.clip(jax.random.uniform(key_of[2], (NBLK, BLOCK, D), jnp.float32, -1.5, 1.5) * block_scale(key_of[2], (NBLK, BLOCK, D), ((1, 16),), -0.4, 0.0), -1.5, 1.5).astype(jnp.bfloat16),
        "cotangent": scatter_about(key_of[3], (SEQS, NBLK, BLOCK, D), 1.0, 6.0, ((0, 2), (1, 16))),
        "block_one": scatter_about(key_of[4], (NBLK, BLOCK, BLOCK), BLOCK ** -0.5, 0.25, ((0, 16),)),
        "block_two": scatter_about(key_of[5], (BLOCK, NBLK, NBLK), NBLK ** -0.5, 0.375, ((0, 16),)),
    }


def product(form, left, right):
    return jnp.einsum(form, left.astype(jnp.float32), right.astype(jnp.float32), precision=lax.Precision.HIGHEST)


def reference(inputs, gate_logits, kernel, cotangent, block_one, block_two):
    kernel_wide = kernel.astype(jnp.float32)

    def one_sequence(totals, slices):
        tokens, gate_one, incoming = slices
        first = product('acb,abd->acd', block_one, tokens).astype(jnp.bfloat16)
        second = product('cea,acd->ecd', block_two, first)
        filtered = (kernel_wide * second).astype(jnp.bfloat16)
        third = product('cef,ecd->fcd', block_two, filtered).astype(jnp.bfloat16)
        fourth = product('fch,fcd->fhd', block_one, third).astype(jnp.bfloat16)
        opened = jax.nn.sigmoid(gate_one.astype(jnp.float32))
        incoming_wide = incoming.astype(jnp.float32)
        fourth_wide = fourth.astype(jnp.float32)
        output = (opened * fourth_wide).astype(jnp.bfloat16)
        grad_gate = (incoming_wide * fourth_wide * opened * (1.0 - opened)).astype(jnp.bfloat16)
        grad_fourth = (incoming_wide * opened).astype(jnp.bfloat16)
        grad_third = product('fch,fhd->fcd', block_one, grad_fourth).astype(jnp.bfloat16)
        grad_filtered = product('cef,fcd->ecd', block_two, grad_third)
        grad_second = (kernel_wide * grad_filtered).astype(jnp.bfloat16)
        grad_first = product('cea,ecd->acd', block_two, grad_second).astype(jnp.bfloat16)
        grad_tokens = product('acb,acd->abd', block_one, grad_first).astype(jnp.bfloat16)
        partials = (
            product('acd,abd->acb', grad_first, tokens) + product('fhd,fcd->fch', grad_fourth, third),
            product('ecd,acd->cea', grad_second, first) + product('fcd,ecd->cef', grad_third, filtered),
            grad_filtered * second,
        )
        totals = tuple(total + part for total, part in zip(totals, partials))
        return totals, (output, grad_tokens, grad_gate)

    start = (
        jnp.zeros((NBLK, BLOCK, BLOCK), jnp.float32),
        jnp.zeros((BLOCK, NBLK, NBLK), jnp.float32),
        jnp.zeros((NBLK, BLOCK, D), jnp.float32),
    )
    totals, stacked = lax.scan(one_sequence, start, (inputs, gate_logits, cotangent))
    output, grad_inputs, grad_gate = stacked
    grad_scale = (SEQS * D) ** -0.5
    grad_kernel = totals[2].astype(jnp.bfloat16)
    grad_block_one = (totals[0] * grad_scale).astype(jnp.bfloat16)
    grad_block_two = (totals[1] * grad_scale).astype(jnp.bfloat16)
    return (output, grad_inputs, grad_gate, grad_kernel, grad_block_one, grad_block_two)
```

```python
import jax
import jax.numpy as jnp
from jax import lax
from jax.sharding import PartitionSpec as P


def to_cols(x):
    return lax.all_to_all(x, "seq", split_axis=1, concat_axis=0, tiled=True)


def to_rows(x):
    return lax.all_to_all(x, "seq", split_axis=0, concat_axis=1, tiled=True)


def held(x):
    return lax.optimization_barrier(x)


def body(inputs, gate_logits, kernel, cotangent, block_one, block_two):
    tokens = inputs[0]
    kernel_wide = kernel.astype(jnp.float32)
    grad_scale = (lax.axis_size("dp") * tokens.shape[2]) ** (-0.5)
    f32 = jnp.float32

    opened = jax.nn.sigmoid(gate_logits[0].astype(f32))
    incoming = cotangent[0].astype(f32)
    grad_fourth = held((incoming * opened).astype(jnp.bfloat16))
    grad_third = jnp.einsum(
        "fch,fhd->fcd", block_one, grad_fourth, preferred_element_type=f32
    ).astype(jnp.bfloat16)
    grad_third_cols = to_cols(held(grad_third))

    first = jnp.einsum(
        "acb,abd->acd", block_one, tokens, preferred_element_type=f32
    ).astype(jnp.bfloat16)
    first, grad_third_cols = held((first, grad_third_cols))
    first_cols = to_cols(first)

    grad_filtered = held(
        jnp.einsum("cef,fcd->ecd", block_two, grad_third_cols, preferred_element_type=f32)
    )
    grad_second = (kernel_wide * grad_filtered).astype(jnp.bfloat16)
    grad_first = jnp.einsum(
        "cea,ecd->acd", block_two, grad_second, preferred_element_type=f32
    ).astype(jnp.bfloat16)
    grad_first, first_cols = held((grad_first, first_cols))
    grad_first_rows = to_rows(grad_first)

    second = held(
        jnp.einsum("cea,acd->ecd", block_two, first_cols, preferred_element_type=f32)
    )
    filtered = (kernel_wide * second).astype(jnp.bfloat16)
    third = jnp.einsum(
        "cef,ecd->fcd", block_two, filtered, preferred_element_type=f32
    ).astype(jnp.bfloat16)
    third, grad_first_rows = held((third, grad_first_rows))
    third_rows = to_rows(third)

    grad_kernel = (grad_filtered * second).astype(jnp.bfloat16)
    grad_block_two = (
        (
            jnp.einsum("fcd,ecd->cef", grad_third_cols, filtered, preferred_element_type=f32)
            + jnp.einsum("ecd,acd->cea", grad_second, first_cols, preferred_element_type=f32)
        )
        * grad_scale
    ).astype(jnp.bfloat16)
    grad_kernel = lax.psum_scatter(grad_kernel, "dp", scatter_dimension=2, tiled=True)
    grad_block_two = lax.psum_scatter(grad_block_two, "dp", scatter_dimension=2, tiled=True)

    grad_tokens = jnp.einsum(
        "acb,acd->abd", block_one, grad_first_rows, preferred_element_type=f32
    ).astype(jnp.bfloat16)
    outer_inputs = jnp.einsum(
        "acd,abd->acb", grad_first_rows, tokens, preferred_element_type=f32
    )

    fourth = jnp.einsum(
        "fch,fcd->fhd", block_one, third_rows, preferred_element_type=f32
    ).astype(jnp.bfloat16)
    fourth_wide = fourth.astype(f32)
    output = (opened * fourth_wide).astype(jnp.bfloat16)
    grad_gate = (incoming * fourth_wide * opened * (1.0 - opened)).astype(jnp.bfloat16)
    outer_one = jnp.einsum(
        "fhd,fcd->fch", grad_fourth, third_rows, preferred_element_type=f32
    )
    grad_block_one = ((outer_one + outer_inputs) * grad_scale).astype(jnp.bfloat16)
    grad_block_one = lax.psum_scatter(grad_block_one, "dp", scatter_dimension=2, tiled=True)
    return (
        output[None],
        grad_tokens[None],
        grad_gate[None],
        grad_kernel,
        grad_block_one,
        grad_block_two,
    )


def solution(mesh):
    return jax.shard_map(
        body,
        mesh=mesh,
        in_specs=(
            P("dp", "seq", None, None),
            P("dp", "seq", None, None),
            P(None, "seq", None),
            P("dp", "seq", None, None),
            P("seq", None, None),
            P("seq", None, None),
        ),
        out_specs=(
            P("dp", "seq", None, None),
            P("dp", "seq", None, None),
            P("dp", "seq", None, None),
            P(None, "seq", "dp"),
            P("seq", None, "dp"),
            P("seq", None, "dp"),
        ),
        check_vma=False,
    )
```

```python
import jax
import jax.numpy as jnp
from jax import lax
from jax.sharding import PartitionSpec as P


def to_cols(x):
    return lax.all_to_all(x, "seq", split_axis=1, concat_axis=0, tiled=True)


def to_rows(x):
    return lax.all_to_all(x, "seq", split_axis=0, concat_axis=1, tiled=True)


def held(x):
    return lax.optimization_barrier(x)


def dp_reduce_scatter(x, dim):
    n = lax.axis_size("dp")
    me = lax.axis_index("dp")
    size = x.shape[dim] // n
    total = lax.dynamic_slice_in_dim(x, me * size, size, axis=dim)
    for shift in range(1, n):
        target = lax.rem(me + shift, n)
        part = lax.dynamic_slice_in_dim(x, target * size, size, axis=dim)
        total = total + lax.ppermute(
            part.astype(jnp.bfloat16),
            "dp",
            [(i, (i + shift) % n) for i in range(n)],
        ).astype(jnp.float32)
    return total.astype(jnp.bfloat16)


def body(inputs, gate_logits, kernel, cotangent, block_one, block_two):
    tokens = inputs[0]
    kernel_wide = kernel.astype(jnp.float32)
    grad_scale = (lax.axis_size("dp") * tokens.shape[2]) ** (-0.5)
    f32 = jnp.float32

    opened = jax.nn.sigmoid(gate_logits[0].astype(f32))
    incoming = cotangent[0].astype(f32)
    grad_fourth = held((incoming * opened).astype(jnp.bfloat16))
    grad_third = jnp.einsum(
        "fch,fhd->fcd", block_one, grad_fourth, preferred_element_type=f32
    ).astype(jnp.bfloat16)
    grad_third_cols = to_cols(held(grad_third))

    first = jnp.einsum(
        "acb,abd->acd", block_one, tokens, preferred_element_type=f32
    ).astype(jnp.bfloat16)
    first, grad_third_cols = held((first, grad_third_cols))
    first_cols = to_cols(first)

    grad_filtered = held(
        jnp.einsum("cef,fcd->ecd", block_two, grad_third_cols, preferred_element_type=f32)
    )
    grad_second = (kernel_wide * grad_filtered).astype(jnp.bfloat16)
    grad_first = jnp.einsum(
        "cea,ecd->acd", block_two, grad_second, preferred_element_type=f32
    ).astype(jnp.bfloat16)
    grad_first, first_cols = held((grad_first, first_cols))
    grad_first_rows = to_rows(grad_first)

    second = held(
        jnp.einsum("cea,acd->ecd", block_two, first_cols, preferred_element_type=f32)
    )
    filtered = (kernel_wide * second).astype(jnp.bfloat16)
    third = jnp.einsum(
        "cef,ecd->fcd", block_two, filtered, preferred_element_type=f32
    ).astype(jnp.bfloat16)
    n_seq = lax.axis_size("seq")
    own = third.shape[0] // n_seq
    half = own // 2
    halves = ((0, half), (half, own)) if half else ((0, own),)
    third_split = third.reshape((n_seq, own) + third.shape[1:])
    third_split, grad_first_rows = held((third_split, grad_first_rows))

    def finish(lo, hi, third_rows):
        fourth = jnp.einsum(
            "fch,fcd->fhd", block_one[lo:hi], third_rows, preferred_element_type=f32
        ).astype(jnp.bfloat16)
        fourth_wide = fourth.astype(f32)
        opened_k = opened[lo:hi]
        output = (opened_k * fourth_wide).astype(jnp.bfloat16)
        grad_gate = (
            incoming[lo:hi] * fourth_wide * opened_k * (1.0 - opened_k)
        ).astype(jnp.bfloat16)
        outer_one = jnp.einsum(
            "fhd,fcd->fch", grad_fourth[lo:hi], third_rows, preferred_element_type=f32
        )
        partial = (outer_one + outer_inputs[lo:hi]) * grad_scale
        return output, grad_gate, dp_reduce_scatter(partial, 2)

    grad_kernel = (grad_filtered * second).astype(jnp.bfloat16)
    grad_block_two = (
        (
            jnp.einsum("fcd,ecd->cef", grad_third_cols, filtered, preferred_element_type=f32)
            + jnp.einsum("ecd,acd->cea", grad_second, first_cols, preferred_element_type=f32)
        )
        * grad_scale
    ).astype(jnp.bfloat16)
    grad_kernel = lax.psum_scatter(grad_kernel, "dp", scatter_dimension=2, tiled=True)
    grad_block_two = lax.psum_scatter(grad_block_two, "dp", scatter_dimension=2, tiled=True)

    grad_tokens = jnp.einsum(
        "acb,acd->abd", block_one, grad_first_rows, preferred_element_type=f32
    ).astype(jnp.bfloat16)
    outer_inputs = jnp.einsum(
        "acd,abd->acb", grad_first_rows, tokens, preferred_element_type=f32
    )

    outputs, grad_gates, grad_block_ones = [], [], []
    pending = None
    for lo, hi in halves:
        piece = third_split[:, lo:hi].reshape((-1,) + third.shape[1:])
        if pending is not None:
            piece, arrived = held((piece, pending[2]))
            outputs_k = finish(pending[0], pending[1], arrived)
            outputs.append(outputs_k[0])
            grad_gates.append(outputs_k[1])
            grad_block_ones.append(outputs_k[2])
        pending = (lo, hi, to_rows(piece))
    outputs_k = finish(*pending)
    outputs.append(outputs_k[0])
    grad_gates.append(outputs_k[1])
    grad_block_ones.append(outputs_k[2])
    output = jnp.concatenate(outputs, axis=0)
    grad_gate = jnp.concatenate(grad_gates, axis=0)
    grad_block_one = jnp.concatenate(grad_block_ones, axis=0)
    return (
        output[None],
        grad_tokens[None],
        grad_gate[None],
        grad_kernel,
        grad_block_one,
        grad_block_two,
    )


def solution(mesh):
    return jax.shard_map(
        body,
        mesh=mesh,
        in_specs=(
            P("dp", "seq", None, None),
            P("dp", "seq", None, None),
            P(None, "seq", None),
            P("dp", "seq", None, None),
            P("seq", None, None),
            P("seq", None, None),
        ),
        out_specs=(
            P("dp", "seq", None, None),
            P("dp", "seq", None, None),
            P("dp", "seq", None, None),
            P(None, "seq", "dp"),
            P("seq", None, "dp"),
            P("seq", None, "dp"),
        ),
        check_vma=False,
    )
```

```python
import jax
import jax.numpy as jnp
from jax import lax
from jax.sharding import PartitionSpec as P


def cols_send(x):
    n = lax.axis_size("seq")
    a, c, d = x.shape
    return x.reshape(a, n, c // n, d).transpose(1, 0, 2, 3)


def cols_recv(x):
    return lax.all_to_all(x, "seq", split_axis=0, concat_axis=0, tiled=True).reshape(
        (-1,) + x.shape[2:]
    )


def to_cols(x):
    return cols_recv(cols_send(x))


def rows_send(x):
    n = lax.axis_size("seq")
    return x.reshape((n, x.shape[0] // n) + x.shape[1:])


def rows_recv(x):
    n, f, c, d = x.shape
    moved = lax.all_to_all(x, "seq", split_axis=0, concat_axis=0, tiled=True)
    return moved.transpose(1, 0, 2, 3).reshape(f, n * c, d)


def held(x):
    return lax.optimization_barrier(x)


def dp_reduce_scatter(x, dim):
    n = lax.axis_size("dp")
    me = lax.axis_index("dp")
    size = x.shape[dim] // n
    total = lax.dynamic_slice_in_dim(x, me * size, size, axis=dim)
    for shift in range(1, n):
        target = lax.rem(me + shift, n)
        part = lax.dynamic_slice_in_dim(x, target * size, size, axis=dim)
        total = total + lax.ppermute(
            part.astype(jnp.bfloat16),
            "dp",
            [(i, (i + shift) % n) for i in range(n)],
        ).astype(jnp.float32)
    return total.astype(jnp.bfloat16)


def body(inputs, gate_logits, kernel, cotangent, block_one, block_two):
    tokens = inputs[0]
    kernel_wide = kernel.astype(jnp.float32)
    grad_scale = (lax.axis_size("dp") * tokens.shape[2]) ** (-0.5)
    f32 = jnp.float32

    opened = jax.nn.sigmoid(gate_logits[0].astype(f32))
    incoming = cotangent[0].astype(f32)
    grad_fourth = held((incoming * opened).astype(jnp.bfloat16))
    grad_third = jnp.einsum(
        "fch,fhd->fcd", block_one, grad_fourth, preferred_element_type=f32
    ).astype(jnp.bfloat16)
    grad_third_cols = cols_recv(held(cols_send(grad_third)))

    first = jnp.einsum(
        "acb,abd->acd", block_one, tokens, preferred_element_type=f32
    ).astype(jnp.bfloat16)
    first_send, grad_third_cols = held((cols_send(first), grad_third_cols))
    first_cols = cols_recv(first_send)

    grad_filtered = held(
        jnp.einsum("cef,fcd->ecd", block_two, grad_third_cols, preferred_element_type=f32)
    )
    grad_second = (kernel_wide * grad_filtered).astype(jnp.bfloat16)
    grad_first = jnp.einsum(
        "cea,ecd->acd", block_two, grad_second, preferred_element_type=f32
    ).astype(jnp.bfloat16)
    grad_first_send, first_cols = held((rows_send(grad_first), first_cols))
    grad_first_rows = rows_recv(grad_first_send)

    second = held(
        jnp.einsum("cea,acd->ecd", block_two, first_cols, preferred_element_type=f32)
    )
    filtered = (kernel_wide * second).astype(jnp.bfloat16)
    third = jnp.einsum(
        "cef,ecd->fcd", block_two, filtered, preferred_element_type=f32
    ).astype(jnp.bfloat16)
    n_seq = lax.axis_size("seq")
    own = third.shape[0] // n_seq
    half = own // 2
    halves = ((0, half), (half, own)) if half else ((0, own),)
    third_split = rows_send(third)
    pieces = [third_split[:, lo:hi] for lo, hi in halves]
    pieces, grad_first_rows = held((pieces, grad_first_rows))

    def finish(lo, hi, third_rows):
        fourth = jnp.einsum(
            "fch,fcd->fhd", block_one[lo:hi], third_rows, preferred_element_type=f32
        ).astype(jnp.bfloat16)
        fourth_wide = fourth.astype(f32)
        opened_k = opened[lo:hi]
        output = (opened_k * fourth_wide).astype(jnp.bfloat16)
        grad_gate = (
            incoming[lo:hi] * fourth_wide * opened_k * (1.0 - opened_k)
        ).astype(jnp.bfloat16)
        outer_one = jnp.einsum(
            "fhd,fcd->fch", grad_fourth[lo:hi], third_rows, preferred_element_type=f32
        )
        partial = (outer_one + outer_inputs[lo:hi]) * grad_scale
        return output, grad_gate, dp_reduce_scatter(partial, 2)

    grad_kernel = (grad_filtered * second).astype(jnp.bfloat16)
    grad_block_two = (
        (
            jnp.einsum("fcd,ecd->cef", grad_third_cols, filtered, preferred_element_type=f32)
            + jnp.einsum("ecd,acd->cea", grad_second, first_cols, preferred_element_type=f32)
        )
        * grad_scale
    ).astype(jnp.bfloat16)
    grad_kernel = lax.psum_scatter(grad_kernel, "dp", scatter_dimension=2, tiled=True)
    grad_block_two = lax.psum_scatter(grad_block_two, "dp", scatter_dimension=2, tiled=True)

    grad_tokens = jnp.einsum(
        "acb,acd->abd", block_one, grad_first_rows, preferred_element_type=f32
    ).astype(jnp.bfloat16)
    outer_inputs = jnp.einsum(
        "acd,abd->acb", grad_first_rows, tokens, preferred_element_type=f32
    )

    outputs, grad_gates, grad_block_ones = [], [], []
    pending = None
    for (lo, hi), piece in zip(halves, pieces):
        if pending is not None:
            piece, arrived = held((piece, pending[2]))
            outputs_k = finish(pending[0], pending[1], arrived)
            outputs.append(outputs_k[0])
            grad_gates.append(outputs_k[1])
            grad_block_ones.append(outputs_k[2])
        pending = (lo, hi, rows_recv(piece))
    outputs_k = finish(*pending)
    outputs.append(outputs_k[0])
    grad_gates.append(outputs_k[1])
    grad_block_ones.append(outputs_k[2])
    output = jnp.concatenate(outputs, axis=0)
    grad_gate = jnp.concatenate(grad_gates, axis=0)
    grad_block_one = jnp.concatenate(grad_block_ones, axis=0)
    return (
        output[None],
        grad_tokens[None],
        grad_gate[None],
        grad_kernel,
        grad_block_one,
        grad_block_two,
    )


def solution(mesh):
    return jax.shard_map(
        body,
        mesh=mesh,
        in_specs=(
            P("dp", "seq", None, None),
            P("dp", "seq", None, None),
            P(None, "seq", None),
            P("dp", "seq", None, None),
            P("seq", None, None),
            P("seq", None, None),
        ),
        out_specs=(
            P("dp", "seq", None, None),
            P("dp", "seq", None, None),
            P("dp", "seq", None, None),
            P(None, "seq", "dp"),
            P("seq", None, "dp"),
            P("seq", None, "dp"),
        ),
        check_vma=False,
    )
```

```python
import jax
import jax.numpy as jnp
from jax import lax
from jax.sharding import PartitionSpec as P
from jax.experimental.layout import Layout, with_layout_constraint


def natural(x):
    return with_layout_constraint(x, Layout(tuple(range(x.ndim))))


def cols_send(x):
    n = lax.axis_size("seq")
    a, c, d = x.shape
    return x.reshape(a, n, c // n, d).transpose(1, 0, 2, 3)


def cols_recv(x):
    return lax.all_to_all(x, "seq", split_axis=0, concat_axis=0, tiled=True).reshape(
        (-1,) + x.shape[2:]
    )


def to_cols(x):
    return cols_recv(cols_send(x))


def rows_send(x):
    n = lax.axis_size("seq")
    return x.reshape((n, x.shape[0] // n) + x.shape[1:])


def rows_recv(x):
    n, f, c, d = x.shape
    moved = lax.all_to_all(x, "seq", split_axis=0, concat_axis=0, tiled=True)
    return moved.transpose(1, 0, 2, 3).reshape(f, n * c, d)


def held(x):
    return lax.optimization_barrier(x)


def dp_reduce_scatter(x, dim):
    n = lax.axis_size("dp")
    me = lax.axis_index("dp")
    size = x.shape[dim] // n
    total = lax.dynamic_slice_in_dim(x, me * size, size, axis=dim)
    for shift in range(1, n):
        target = lax.rem(me + shift, n)
        part = lax.dynamic_slice_in_dim(x, target * size, size, axis=dim)
        total = total + lax.ppermute(
            part.astype(jnp.bfloat16),
            "dp",
            [(i, (i + shift) % n) for i in range(n)],
        ).astype(jnp.float32)
    return total.astype(jnp.bfloat16)


def body(inputs, gate_logits, kernel, cotangent, block_one, block_two):
    tokens = inputs[0]
    kernel_wide = kernel.astype(jnp.float32)
    grad_scale = (lax.axis_size("dp") * tokens.shape[2]) ** (-0.5)
    f32 = jnp.float32

    opened = jax.nn.sigmoid(gate_logits[0].astype(f32))
    incoming = cotangent[0].astype(f32)
    grad_fourth = held((incoming * opened).astype(jnp.bfloat16))
    grad_third = jnp.einsum(
        "fch,fhd->fcd", block_one, grad_fourth, preferred_element_type=f32
    ).astype(jnp.bfloat16)
    grad_third_cols = cols_recv(held(cols_send(grad_third)))

    first = jnp.einsum(
        "acb,abd->acd", block_one, tokens, preferred_element_type=f32
    ).astype(jnp.bfloat16)
    first_send, grad_third_cols = held((cols_send(first), grad_third_cols))
    first_cols = cols_recv(first_send)

    grad_filtered = held(
        jnp.einsum("cef,fcd->ecd", block_two, grad_third_cols, preferred_element_type=f32)
    )
    grad_second = (kernel_wide * grad_filtered).astype(jnp.bfloat16)
    grad_first = jnp.einsum(
        "cea,ecd->acd", block_two, grad_second, preferred_element_type=f32
    ).astype(jnp.bfloat16)
    grad_first_send, first_cols = held((rows_send(grad_first), first_cols))
    grad_first_rows = rows_recv(grad_first_send)

    second = held(
        jnp.einsum("cea,acd->ecd", block_two, first_cols, preferred_element_type=f32)
    )
    filtered = (kernel_wide * second).astype(jnp.bfloat16)
    third = jnp.einsum(
        "cef,ecd->fcd", block_two, filtered, preferred_element_type=f32
    ).astype(jnp.bfloat16)
    n_seq = lax.axis_size("seq")
    own = third.shape[0] // n_seq
    half = own // 2
    halves = ((0, half), (half, own)) if half else ((0, own),)
    third_split = rows_send(third)
    pieces = [third_split[:, lo:hi] for lo, hi in halves]
    pieces, grad_first_rows = held((pieces, grad_first_rows))

    def finish(lo, hi, third_rows):
        fourth = jnp.einsum(
            "fch,fcd->fhd", block_one[lo:hi], third_rows, preferred_element_type=f32
        ).astype(jnp.bfloat16)
        fourth_wide = natural(fourth).astype(f32)
        opened_k = opened[lo:hi]
        output = (opened_k * fourth_wide).astype(jnp.bfloat16)
        grad_gate = (
            incoming[lo:hi] * fourth_wide * opened_k * (1.0 - opened_k)
        ).astype(jnp.bfloat16)
        outer_one = jnp.einsum(
            "fhd,fcd->fch", grad_fourth[lo:hi], third_rows, preferred_element_type=f32
        )
        partial = (outer_one + outer_inputs[lo:hi]) * grad_scale
        return output, grad_gate, dp_reduce_scatter(partial, 2)

    grad_kernel = (grad_filtered * second).astype(jnp.bfloat16)
    grad_block_two = (
        (
            jnp.einsum("fcd,ecd->cef", grad_third_cols, filtered, preferred_element_type=f32)
            + jnp.einsum("ecd,acd->cea", grad_second, first_cols, preferred_element_type=f32)
        )
        * grad_scale
    ).astype(jnp.bfloat16)
    grad_kernel = lax.psum_scatter(grad_kernel, "dp", scatter_dimension=2, tiled=True)
    grad_block_two = lax.psum_scatter(grad_block_two, "dp", scatter_dimension=2, tiled=True)

    grad_tokens = jnp.einsum(
        "acb,acd->abd", block_one, grad_first_rows, preferred_element_type=f32
    ).astype(jnp.bfloat16)
    outer_inputs = jnp.einsum(
        "acd,abd->acb", grad_first_rows, tokens, preferred_element_type=f32
    )

    outputs, grad_gates, grad_block_ones = [], [], []
    pending = None
    for (lo, hi), piece in zip(halves, pieces):
        if pending is not None:
            piece, arrived = held((piece, pending[2]))
            outputs_k = finish(pending[0], pending[1], arrived)
            outputs.append(outputs_k[0])
            grad_gates.append(outputs_k[1])
            grad_block_ones.append(outputs_k[2])
        pending = (lo, hi, rows_recv(piece))
    outputs_k = finish(*pending)
    outputs.append(outputs_k[0])
    grad_gates.append(outputs_k[1])
    grad_block_ones.append(outputs_k[2])
    output = jnp.concatenate(outputs, axis=0)
    grad_gate = jnp.concatenate(grad_gates, axis=0)
    grad_block_one = jnp.concatenate(grad_block_ones, axis=0)
    return (
        output[None],
        grad_tokens[None],
        grad_gate[None],
        grad_kernel,
        grad_block_one,
        grad_block_two,
    )


def solution(mesh):
    return jax.shard_map(
        body,
        mesh=mesh,
        in_specs=(
            P("dp", "seq", None, None),
            P("dp", "seq", None, None),
            P(None, "seq", None),
            P("dp", "seq", None, None),
            P("seq", None, None),
            P("seq", None, None),
        ),
        out_specs=(
            P("dp", "seq", None, None),
            P("dp", "seq", None, None),
            P("dp", "seq", None, None),
            P(None, "seq", "dp"),
            P("seq", None, "dp"),
            P("seq", None, "dp"),
        ),
        check_vma=False,
    )
```

```python
import jax
import jax.numpy as jnp
from jax import lax
from jax.sharding import PartitionSpec as P
from jax.experimental.layout import Layout, with_layout_constraint


def natural(x):
    return with_layout_constraint(x, Layout(tuple(range(x.ndim))))


def cols_send(x):
    n = lax.axis_size("seq")
    a, c, d = x.shape
    return x.reshape(a, n, c // n, d).transpose(1, 0, 2, 3)


def cols_recv(x):
    return lax.all_to_all(x, "seq", split_axis=0, concat_axis=0, tiled=True).reshape(
        (-1,) + x.shape[2:]
    )


def to_cols(x):
    return cols_recv(cols_send(x))


def rows_send(x):
    n = lax.axis_size("seq")
    return x.reshape((n, x.shape[0] // n) + x.shape[1:])


def rows_recv(x):
    n, f, c, d = x.shape
    moved = lax.all_to_all(x, "seq", split_axis=0, concat_axis=0, tiled=True)
    return moved.transpose(1, 0, 2, 3).reshape(f, n * c, d)


def held(x):
    return lax.optimization_barrier(x)


def dp_reduce_scatter(x, dim):
    n = lax.axis_size("dp")
    me = lax.axis_index("dp")
    size = x.shape[dim] // n
    total = lax.dynamic_slice_in_dim(x, me * size, size, axis=dim)
    for shift in range(1, n):
        target = lax.rem(me + shift, n)
        part = lax.dynamic_slice_in_dim(x, target * size, size, axis=dim)
        total = total + lax.ppermute(
            part.astype(jnp.bfloat16),
            "dp",
            [(i, (i + shift) % n) for i in range(n)],
        ).astype(jnp.float32)
    return total.astype(jnp.bfloat16)


def body(inputs, gate_logits, kernel, cotangent, block_one, block_two):
    tokens = inputs[0]
    kernel_wide = kernel.astype(jnp.float32)
    grad_scale = (lax.axis_size("dp") * tokens.shape[2]) ** (-0.5)
    f32 = jnp.float32
    n_seq = lax.axis_size("seq")

    first = jnp.einsum(
        "acb,abd->acd", block_one, tokens, preferred_element_type=f32
    ).astype(jnp.bfloat16)
    first_cols = cols_recv(held(cols_send(first)))

    opened = jax.nn.sigmoid(gate_logits[0].astype(f32))
    incoming = cotangent[0].astype(f32)
    grad_fourth = held((incoming * opened).astype(jnp.bfloat16))
    grad_third = jnp.einsum(
        "fch,fhd->fcd", block_one, grad_fourth, preferred_element_type=f32
    ).astype(jnp.bfloat16)
    grad_third_send, first_cols = held((cols_send(grad_third), first_cols))
    grad_third_cols = cols_recv(grad_third_send)

    second = held(
        jnp.einsum("cea,acd->ecd", block_two, first_cols, preferred_element_type=f32)
    )
    filtered = (kernel_wide * second).astype(jnp.bfloat16)
    third = jnp.einsum(
        "cef,ecd->fcd", block_two, filtered, preferred_element_type=f32
    ).astype(jnp.bfloat16)
    third_send, grad_third_cols = held((rows_send(third), grad_third_cols))
    third_rows = rows_recv(third_send)

    grad_filtered = held(
        jnp.einsum("cef,fcd->ecd", block_two, grad_third_cols, preferred_element_type=f32)
    )
    grad_second = (kernel_wide * grad_filtered).astype(jnp.bfloat16)
    grad_first = jnp.einsum(
        "cea,ecd->acd", block_two, grad_second, preferred_element_type=f32
    ).astype(jnp.bfloat16)

    grad_kernel = (grad_filtered * second).astype(jnp.bfloat16)
    grad_block_two = (
        (
            jnp.einsum("fcd,ecd->cef", grad_third_cols, filtered, preferred_element_type=f32)
            + jnp.einsum("ecd,acd->cea", grad_second, first_cols, preferred_element_type=f32)
        )
        * grad_scale
    ).astype(jnp.bfloat16)
    grad_kernel = lax.psum_scatter(grad_kernel, "dp", scatter_dimension=2, tiled=True)
    grad_block_two = lax.psum_scatter(grad_block_two, "dp", scatter_dimension=2, tiled=True)

    own = grad_first.shape[0] // n_seq
    half = own // 2
    halves = ((0, half), (half, own)) if half else ((0, own),)
    grad_first_split = rows_send(grad_first)
    pieces = [grad_first_split[:, lo:hi] for lo, hi in halves]
    pieces, third_rows = held((pieces, third_rows))

    fourth = jnp.einsum(
        "fch,fcd->fhd", block_one, third_rows, preferred_element_type=f32
    ).astype(jnp.bfloat16)
    fourth_wide = natural(fourth).astype(f32)
    output = (opened * fourth_wide).astype(jnp.bfloat16)
    grad_gate = (incoming * fourth_wide * opened * (1.0 - opened)).astype(jnp.bfloat16)
    outer_one = jnp.einsum(
        "fhd,fcd->fch", grad_fourth, third_rows, preferred_element_type=f32
    )

    def finish(lo, hi, grad_first_rows):
        grad_tokens = natural(
            jnp.einsum(
                "acb,acd->abd", block_one[lo:hi], grad_first_rows, preferred_element_type=f32
            ).astype(jnp.bfloat16)
        )
        outer_inputs = jnp.einsum(
            "acd,abd->acb", grad_first_rows, tokens[lo:hi], preferred_element_type=f32
        )
        partial = (outer_one[lo:hi] + outer_inputs) * grad_scale
        return grad_tokens, dp_reduce_scatter(partial, 2)

    grad_tokens_parts, grad_block_ones = [], []
    pending = None
    for (lo, hi), piece in zip(halves, pieces):
        if pending is not None:
            piece, arrived = held((piece, pending[2]))
            done = finish(pending[0], pending[1], arrived)
            grad_tokens_parts.append(done[0])
            grad_block_ones.append(done[1])
        pending = (lo, hi, rows_recv(piece))
    arrived, grad_tokens_parts, output, grad_gate = held(
        (pending[2], grad_tokens_parts, output, grad_gate)
    )
    done = finish(pending[0], pending[1], arrived)
    grad_tokens_parts.append(done[0])
    grad_block_ones.append(done[1])
    grad_tokens = jnp.concatenate(grad_tokens_parts, axis=0)
    grad_block_one = jnp.concatenate(grad_block_ones, axis=0)
    return (
        output[None],
        grad_tokens[None],
        grad_gate[None],
        grad_kernel,
        grad_block_one,
        grad_block_two,
    )


def solution(mesh):
    return jax.shard_map(
        body,
        mesh=mesh,
        in_specs=(
            P("dp", "seq", None, None),
            P("dp", "seq", None, None),
            P(None, "seq", None),
            P("dp", "seq", None, None),
            P("seq", None, None),
            P("seq", None, None),
        ),
        out_specs=(
            P("dp", "seq", None, None),
            P("dp", "seq", None, None),
            P("dp", "seq", None, None),
            P(None, "seq", "dp"),
            P("seq", None, "dp"),
            P("seq", None, "dp"),
        ),
        check_vma=False,
    )
```

```python
import jax
import jax.numpy as jnp
from jax import lax
from jax.sharding import PartitionSpec as P
from jax.experimental.layout import Layout, with_layout_constraint


def natural(x):
    return with_layout_constraint(x, Layout(tuple(range(x.ndim))))


def cols_send(x):
    n = lax.axis_size("seq")
    a, c, d = x.shape
    return x.reshape(a, n, c // n, d).transpose(1, 0, 2, 3)


def cols_recv(x):
    return lax.all_to_all(x, "seq", split_axis=0, concat_axis=0, tiled=True).reshape(
        (-1,) + x.shape[2:]
    )


def to_cols(x):
    return cols_recv(cols_send(x))


def rows_send(x):
    n = lax.axis_size("seq")
    return x.reshape((n, x.shape[0] // n) + x.shape[1:])


def rows_recv(x):
    n, f, c, d = x.shape
    moved = lax.all_to_all(x, "seq", split_axis=0, concat_axis=0, tiled=True)
    return moved.transpose(1, 0, 2, 3).reshape(f, n * c, d)


def held(x):
    return lax.optimization_barrier(x)


def dp_reduce_scatter(x, dim):
    n = lax.axis_size("dp")
    me = lax.axis_index("dp")
    size = x.shape[dim] // n
    total = lax.dynamic_slice_in_dim(x, me * size, size, axis=dim)
    for shift in range(1, n):
        target = lax.rem(me + shift, n)
        part = lax.dynamic_slice_in_dim(x, target * size, size, axis=dim)
        total = total + lax.ppermute(
            part.astype(jnp.bfloat16),
            "dp",
            [(i, (i + shift) % n) for i in range(n)],
        ).astype(jnp.float32)
    return total.astype(jnp.bfloat16)


def body(inputs, gate_logits, kernel, cotangent, block_one, block_two):
    tokens = inputs[0]
    kernel_wide = kernel.astype(jnp.float32)
    grad_scale = (lax.axis_size("dp") * tokens.shape[2]) ** (-0.5)
    f32 = jnp.float32
    n_seq = lax.axis_size("seq")

    first = jnp.einsum(
        "acb,abd->acd", block_one, tokens, preferred_element_type=f32
    ).astype(jnp.bfloat16)
    first_cols = cols_recv(held(cols_send(first)))

    opened = jax.nn.sigmoid(gate_logits[0].astype(f32))
    incoming = cotangent[0].astype(f32)
    grad_fourth = held((incoming * opened).astype(jnp.bfloat16))
    grad_third = jnp.einsum(
        "fch,fhd->fcd", block_one, grad_fourth, preferred_element_type=f32
    ).astype(jnp.bfloat16)
    grad_third_send, first_cols = held((cols_send(grad_third), first_cols))
    grad_third_cols = cols_recv(grad_third_send)

    second = held(
        jnp.einsum("cea,acd->ecd", block_two, first_cols, preferred_element_type=f32)
    )
    filtered = (kernel_wide * second).astype(jnp.bfloat16)
    third = jnp.einsum(
        "cef,ecd->fcd", block_two, filtered, preferred_element_type=f32
    ).astype(jnp.bfloat16)
    third_send, grad_third_cols = held((rows_send(third), grad_third_cols))
    third_rows = rows_recv(third_send)

    grad_filtered = held(
        jnp.einsum("cef,fcd->ecd", block_two, grad_third_cols, preferred_element_type=f32)
    )
    grad_second = (kernel_wide * grad_filtered).astype(jnp.bfloat16)
    grad_first = jnp.einsum(
        "cea,ecd->acd", block_two, grad_second, preferred_element_type=f32
    ).astype(jnp.bfloat16)

    grad_kernel = (grad_filtered * second).astype(jnp.bfloat16)
    grad_block_two = (
        (
            jnp.einsum("fcd,ecd->cef", grad_third_cols, filtered, preferred_element_type=f32)
            + jnp.einsum("ecd,acd->cea", grad_second, first_cols, preferred_element_type=f32)
        )
        * grad_scale
    ).astype(jnp.bfloat16)
    grad_kernel = lax.psum_scatter(grad_kernel, "dp", scatter_dimension=2, tiled=True)
    grad_block_two = lax.psum_scatter(grad_block_two, "dp", scatter_dimension=2, tiled=True)

    own = grad_first.shape[0] // n_seq
    half = own // 2
    halves = ((0, half), (half, own)) if half else ((0, own),)
    grad_first_split = rows_send(grad_first)
    pieces = [grad_first_split[:, lo:hi] for lo, hi in halves]
    pieces, third_rows = held((pieces, third_rows))

    fourth = jnp.einsum(
        "fch,fcd->fhd", block_one, third_rows, preferred_element_type=f32
    ).astype(jnp.bfloat16)
    fourth_wide = natural(fourth).astype(f32)
    output = (opened * fourth_wide).astype(jnp.bfloat16)
    grad_gate = (incoming * fourth_wide * opened * (1.0 - opened)).astype(jnp.bfloat16)
    outer_one = jnp.einsum(
        "fhd,fcd->fch", grad_fourth, third_rows, preferred_element_type=f32
    )

    def finish(lo, hi, grad_first_rows):
        grad_tokens = natural(
            jnp.einsum(
                "acb,acd->abd", block_one[lo:hi], grad_first_rows, preferred_element_type=f32
            ).astype(jnp.bfloat16)
        )
        outer_inputs = jnp.einsum(
            "acd,abd->acb", grad_first_rows, tokens[lo:hi], preferred_element_type=f32
        )
        partial = (outer_one[lo:hi] + outer_inputs) * grad_scale
        return grad_tokens, dp_reduce_scatter(partial, 2)

    grad_tokens_parts, grad_block_ones = [], []
    pending = None
    for (lo, hi), piece in zip(halves, pieces):
        if pending is not None:
            piece, arrived, (output, grad_gate, outer_one) = held(
                (piece, pending[2], (output, grad_gate, outer_one))
            )
            done = finish(pending[0], pending[1], arrived)
            grad_tokens_parts.append(done[0])
            grad_block_ones.append(done[1])
        pending = (lo, hi, rows_recv(piece))
    arrived, grad_tokens_parts, output, grad_gate = held(
        (pending[2], grad_tokens_parts, output, grad_gate)
    )
    done = finish(pending[0], pending[1], arrived)
    grad_tokens_parts.append(done[0])
    grad_block_ones.append(done[1])
    grad_tokens = jnp.concatenate(grad_tokens_parts, axis=0)
    grad_block_one = jnp.concatenate(grad_block_ones, axis=0)
    return (
        output[None],
        grad_tokens[None],
        grad_gate[None],
        grad_kernel,
        grad_block_one,
        grad_block_two,
    )


def solution(mesh):
    return jax.shard_map(
        body,
        mesh=mesh,
        in_specs=(
            P("dp", "seq", None, None),
            P("dp", "seq", None, None),
            P(None, "seq", None),
            P("dp", "seq", None, None),
            P("seq", None, None),
            P("seq", None, None),
        ),
        out_specs=(
            P("dp", "seq", None, None),
            P("dp", "seq", None, None),
            P("dp", "seq", None, None),
            P(None, "seq", "dp"),
            P("seq", None, "dp"),
            P("seq", None, "dp"),
        ),
        check_vma=False,
    )
```

```python
import jax
import jax.numpy as jnp
from jax import lax
from jax.sharding import PartitionSpec as P
from jax.experimental.layout import Layout, with_layout_constraint


def natural(x):
    return with_layout_constraint(x, Layout(tuple(range(x.ndim))))


def cols_send(x):
    n = lax.axis_size("seq")
    a, c, d = x.shape
    return x.reshape(a, n, c // n, d).transpose(1, 0, 2, 3)


def cols_recv(x):
    return lax.all_to_all(x, "seq", split_axis=0, concat_axis=0, tiled=True).reshape(
        (-1,) + x.shape[2:]
    )


def to_cols(x):
    return cols_recv(cols_send(x))


def rows_send(x):
    n = lax.axis_size("seq")
    return x.reshape((n, x.shape[0] // n) + x.shape[1:])


def rows_recv(x):
    n, f, c, d = x.shape
    moved = lax.all_to_all(x, "seq", split_axis=0, concat_axis=0, tiled=True)
    return moved.transpose(1, 0, 2, 3).reshape(f, n * c, d)


def held(x):
    return lax.optimization_barrier(x)


def dp_reduce_scatter(x, dim):
    n = lax.axis_size("dp")
    me = lax.axis_index("dp")
    size = x.shape[dim] // n
    total = lax.dynamic_slice_in_dim(x, me * size, size, axis=dim)
    for shift in range(1, n):
        target = lax.rem(me + shift, n)
        part = lax.dynamic_slice_in_dim(x, target * size, size, axis=dim)
        total = total + lax.ppermute(
            part.astype(jnp.bfloat16),
            "dp",
            [(i, (i + shift) % n) for i in range(n)],
        ).astype(jnp.float32)
    return total.astype(jnp.bfloat16)


def body(inputs, gate_logits, kernel, cotangent, block_one, block_two):
    tokens = inputs[0]
    kernel_wide = kernel.astype(jnp.float32)
    grad_scale = (lax.axis_size("dp") * tokens.shape[2]) ** (-0.5)
    f32 = jnp.float32
    n_seq = lax.axis_size("seq")

    first = jnp.einsum(
        "acb,abd->acd", block_one, tokens, preferred_element_type=f32
    ).astype(jnp.bfloat16)
    first_cols = cols_recv(held(cols_send(first)))

    opened = jax.nn.sigmoid(gate_logits[0].astype(f32))
    incoming = cotangent[0].astype(f32)
    grad_fourth = held((incoming * opened).astype(jnp.bfloat16))
    grad_third = jnp.einsum(
        "fch,fhd->fcd", block_one, grad_fourth, preferred_element_type=f32
    ).astype(jnp.bfloat16)
    grad_third_send, first_cols = held((cols_send(grad_third), first_cols))
    grad_third_cols = cols_recv(grad_third_send)

    second = held(
        jnp.einsum("cea,acd->ecd", block_two, first_cols, preferred_element_type=f32)
    )
    filtered = (kernel_wide * second).astype(jnp.bfloat16)
    third = jnp.einsum(
        "cef,ecd->fcd", block_two, filtered, preferred_element_type=f32
    ).astype(jnp.bfloat16)
    third_send, grad_third_cols = held((rows_send(third), grad_third_cols))
    third_rows = rows_recv(third_send)

    grad_filtered = held(
        jnp.einsum("cef,fcd->ecd", block_two, grad_third_cols, preferred_element_type=f32)
    )
    grad_second = (kernel_wide * grad_filtered).astype(jnp.bfloat16)
    grad_first = jnp.einsum(
        "cea,ecd->acd", block_two, grad_second, preferred_element_type=f32
    ).astype(jnp.bfloat16)

    grad_kernel = (grad_filtered * second).astype(jnp.bfloat16)
    grad_block_two = (
        (
            jnp.einsum("fcd,ecd->cef", grad_third_cols, filtered, preferred_element_type=f32)
            + jnp.einsum("ecd,acd->cea", grad_second, first_cols, preferred_element_type=f32)
        )
        * grad_scale
    ).astype(jnp.bfloat16)
    grad_kernel = lax.psum_scatter(grad_kernel, "dp", scatter_dimension=2, tiled=True)
    grad_block_two = lax.psum_scatter(grad_block_two, "dp", scatter_dimension=2, tiled=True)

    own = grad_first.shape[0] // n_seq
    cut = 3 * own // 4 if own % 4 == 0 else own // 2
    halves = ((0, cut), (cut, own)) if cut else ((0, own),)
    grad_first_split = rows_send(grad_first)
    pieces = [grad_first_split[:, lo:hi] for lo, hi in halves]
    pieces, third_rows = held((pieces, third_rows))

    fourth = jnp.einsum(
        "fch,fcd->fhd", block_one, third_rows, preferred_element_type=f32
    ).astype(jnp.bfloat16)
    fourth_wide = natural(fourth).astype(f32)
    output = (opened * fourth_wide).astype(jnp.bfloat16)
    grad_gate = (incoming * fourth_wide * opened * (1.0 - opened)).astype(jnp.bfloat16)
    outer_one = jnp.einsum(
        "fhd,fcd->fch", grad_fourth, third_rows, preferred_element_type=f32
    )

    def finish(lo, hi, grad_first_rows):
        grad_tokens = natural(
            jnp.einsum(
                "acb,acd->abd", block_one[lo:hi], grad_first_rows, preferred_element_type=f32
            ).astype(jnp.bfloat16)
        )
        outer_inputs = jnp.einsum(
            "acd,abd->acb", grad_first_rows, tokens[lo:hi], preferred_element_type=f32
        )
        partial = (outer_one[lo:hi] + outer_inputs) * grad_scale
        return grad_tokens, dp_reduce_scatter(partial, 2)

    grad_tokens_parts, grad_block_ones = [], []
    pending = None
    for (lo, hi), piece in zip(halves, pieces):
        if pending is not None:
            piece, arrived, (output, grad_gate, outer_one) = held(
                (piece, pending[2], (output, grad_gate, outer_one))
            )
            done = finish(pending[0], pending[1], arrived)
            grad_tokens_parts.append(done[0])
            grad_block_ones.append(done[1])
        pending = (lo, hi, rows_recv(piece))
    arrived, grad_tokens_parts, output, grad_gate = held(
        (pending[2], grad_tokens_parts, output, grad_gate)
    )
    done = finish(pending[0], pending[1], arrived)
    grad_tokens_parts.append(done[0])
    grad_block_ones.append(done[1])
    grad_tokens = jnp.concatenate(grad_tokens_parts, axis=0)
    grad_block_one = jnp.concatenate(grad_block_ones, axis=0)
    return (
        output[None],
        grad_tokens[None],
        grad_gate[None],
        grad_kernel,
        grad_block_one,
        grad_block_two,
    )


def solution(mesh):
    return jax.shard_map(
        body,
        mesh=mesh,
        in_specs=(
            P("dp", "seq", None, None),
            P("dp", "seq", None, None),
            P(None, "seq", None),
            P("dp", "seq", None, None),
            P("seq", None, None),
            P("seq", None, None),
        ),
        out_specs=(
            P("dp", "seq", None, None),
            P("dp", "seq", None, None),
            P("dp", "seq", None, None),
            P(None, "seq", "dp"),
            P("seq", None, "dp"),
            P("seq", None, "dp"),
        ),
        check_vma=False,
    )
```

```python
import jax
import jax.numpy as jnp
from jax import lax
from jax.sharding import PartitionSpec as P
from jax.experimental.layout import Layout, with_layout_constraint


def natural(x):
    return with_layout_constraint(x, Layout(tuple(range(x.ndim))))


def cols_send(x):
    n = lax.axis_size("seq")
    a, c, d = x.shape
    return x.reshape(a, n, c // n, d).transpose(1, 0, 2, 3)


def cols_recv(x):
    return lax.all_to_all(x, "seq", split_axis=0, concat_axis=0, tiled=True).reshape(
        (-1,) + x.shape[2:]
    )


def to_cols(x):
    return cols_recv(cols_send(x))


def rows_send(x):
    n = lax.axis_size("seq")
    return x.reshape((n, x.shape[0] // n) + x.shape[1:])


def rows_move(x):
    return lax.all_to_all(x, "seq", split_axis=0, concat_axis=0, tiled=True)


def rows_order(x):
    n, f, c, d = x.shape
    return x.transpose(1, 0, 2, 3).reshape(f, n * c, d)


def held(x):
    return lax.optimization_barrier(x)


def dp_reduce_scatter(x, dim):
    n = lax.axis_size("dp")
    me = lax.axis_index("dp")
    size = x.shape[dim] // n
    total = lax.dynamic_slice_in_dim(x, me * size, size, axis=dim)
    for shift in range(1, n):
        target = lax.rem(me + shift, n)
        part = lax.dynamic_slice_in_dim(x, target * size, size, axis=dim)
        total = total + lax.ppermute(
            part.astype(jnp.bfloat16),
            "dp",
            [(i, (i + shift) % n) for i in range(n)],
        ).astype(jnp.float32)
    return total.astype(jnp.bfloat16)


def body(inputs, gate_logits, kernel, cotangent, block_one, block_two):
    tokens = inputs[0]
    kernel_wide = kernel.astype(jnp.float32)
    grad_scale = (lax.axis_size("dp") * tokens.shape[2]) ** (-0.5)
    f32 = jnp.float32
    n_seq = lax.axis_size("seq")

    first = jnp.einsum(
        "acb,abd->acd", block_one, tokens, preferred_element_type=f32
    ).astype(jnp.bfloat16)
    first_cols = cols_recv(held(cols_send(first)))

    opened = jax.nn.sigmoid(gate_logits[0].astype(f32))
    incoming = cotangent[0].astype(f32)
    grad_fourth = held((incoming * opened).astype(jnp.bfloat16))
    grad_third = jnp.einsum(
        "fch,fhd->fcd", block_one, grad_fourth, preferred_element_type=f32
    ).astype(jnp.bfloat16)
    grad_third_send, first_cols = held((cols_send(grad_third), first_cols))
    grad_third_cols = cols_recv(grad_third_send)

    second = held(
        jnp.einsum("cea,acd->ecd", block_two, first_cols, preferred_element_type=f32)
    )
    filtered = (kernel_wide * second).astype(jnp.bfloat16)
    third = jnp.einsum(
        "cef,ecd->fcd", block_two, filtered, preferred_element_type=f32
    ).astype(jnp.bfloat16)
    third_send, grad_third_cols = held((natural(rows_send(third)), grad_third_cols))
    third_arrived = rows_move(third_send)

    grad_filtered = held(
        jnp.einsum("cef,fcd->ecd", block_two, grad_third_cols, preferred_element_type=f32)
    )
    grad_second = (kernel_wide * grad_filtered).astype(jnp.bfloat16)
    grad_first = jnp.einsum(
        "cea,ecd->acd", block_two, grad_second, preferred_element_type=f32
    ).astype(jnp.bfloat16)

    grad_kernel = (grad_filtered * second).astype(jnp.bfloat16)
    grad_block_two = (
        (
            jnp.einsum("fcd,ecd->cef", grad_third_cols, filtered, preferred_element_type=f32)
            + jnp.einsum("ecd,acd->cea", grad_second, first_cols, preferred_element_type=f32)
        )
        * grad_scale
    ).astype(jnp.bfloat16)
    grad_kernel = lax.psum_scatter(grad_kernel, "dp", scatter_dimension=2, tiled=True)
    grad_block_two = lax.psum_scatter(grad_block_two, "dp", scatter_dimension=2, tiled=True)

    own = grad_first.shape[0] // n_seq
    half = own // 2
    halves = ((0, half), (half, own)) if half else ((0, own),)
    grad_first_split = rows_send(grad_first)
    pieces = [grad_first_split[:, lo:hi] for lo, hi in halves]
    pieces, third_arrived = held((pieces, third_arrived))
    third_rows = rows_order(third_arrived)

    fourth = jnp.einsum(
        "fch,fcd->fhd", block_one, third_rows, preferred_element_type=f32
    ).astype(jnp.bfloat16)
    fourth_wide = natural(fourth).astype(f32)
    output = (opened * fourth_wide).astype(jnp.bfloat16)
    grad_gate = (incoming * fourth_wide * opened * (1.0 - opened)).astype(jnp.bfloat16)
    outer_one = jnp.einsum(
        "fhd,fcd->fch", grad_fourth, third_rows, preferred_element_type=f32
    )

    def finish(lo, hi, grad_first_rows):
        grad_tokens = natural(
            jnp.einsum(
                "acb,acd->abd", block_one[lo:hi], grad_first_rows, preferred_element_type=f32
            ).astype(jnp.bfloat16)
        )
        outer_inputs = jnp.einsum(
            "acd,abd->acb", grad_first_rows, tokens[lo:hi], preferred_element_type=f32
        )
        partial = (outer_one[lo:hi] + outer_inputs) * grad_scale
        return grad_tokens, dp_reduce_scatter(partial, 2)

    grad_tokens_parts, grad_block_ones = [], []
    pending = None
    for (lo, hi), piece in zip(halves, pieces):
        if pending is not None:
            piece, arrived, (output, grad_gate, outer_one) = held(
                (piece, pending[2], (output, grad_gate, outer_one))
            )
            done = finish(pending[0], pending[1], rows_order(arrived))
            grad_tokens_parts.append(done[0])
            grad_block_ones.append(done[1])
        pending = (lo, hi, rows_move(piece))
    arrived, grad_tokens_parts, output, grad_gate = held(
        (pending[2], grad_tokens_parts, output, grad_gate)
    )
    done = finish(pending[0], pending[1], rows_order(arrived))
    grad_tokens_parts.append(done[0])
    grad_block_ones.append(done[1])
    grad_tokens = jnp.concatenate(grad_tokens_parts, axis=0)
    grad_block_one = jnp.concatenate(grad_block_ones, axis=0)
    return (
        output[None],
        grad_tokens[None],
        grad_gate[None],
        grad_kernel,
        grad_block_one,
        grad_block_two,
    )


def solution(mesh):
    return jax.shard_map(
        body,
        mesh=mesh,
        in_specs=(
            P("dp", "seq", None, None),
            P("dp", "seq", None, None),
            P(None, "seq", None),
            P("dp", "seq", None, None),
            P("seq", None, None),
            P("seq", None, None),
        ),
        out_specs=(
            P("dp", "seq", None, None),
            P("dp", "seq", None, None),
            P("dp", "seq", None, None),
            P(None, "seq", "dp"),
            P("seq", None, "dp"),
            P("seq", None, "dp"),
        ),
        check_vma=False,
    )
```

```python
import jax
import jax.numpy as jnp
from jax import lax
from jax.sharding import PartitionSpec as P
from jax.experimental.layout import Layout, with_layout_constraint


def natural(x):
    return with_layout_constraint(x, Layout(tuple(range(x.ndim))))


def cols_send(x):
    n = lax.axis_size("seq")
    a, c, d = x.shape
    return x.reshape(a, n, c // n, d).transpose(1, 0, 2, 3)


def cols_recv(x):
    return lax.all_to_all(x, "seq", split_axis=0, concat_axis=0, tiled=True).reshape(
        (-1,) + x.shape[2:]
    )


def to_cols(x):
    return cols_recv(cols_send(x))


def rows_send(x):
    n = lax.axis_size("seq")
    return x.reshape((n, x.shape[0] // n) + x.shape[1:])


def rows_move(x):
    return lax.all_to_all(x, "seq", split_axis=0, concat_axis=0, tiled=True)


def rows_order(x):
    n, f, c, d = x.shape
    return x.transpose(1, 0, 2, 3).reshape(f, n * c, d)


def held(x):
    return lax.optimization_barrier(x)


def dp_reduce_scatter(x, dim):
    n = lax.axis_size("dp")
    me = lax.axis_index("dp")
    size = x.shape[dim] // n
    total = lax.dynamic_slice_in_dim(x, me * size, size, axis=dim)
    for shift in range(1, n):
        target = lax.rem(me + shift, n)
        part = lax.dynamic_slice_in_dim(x, target * size, size, axis=dim)
        total = total + lax.ppermute(
            part.astype(jnp.bfloat16),
            "dp",
            [(i, (i + shift) % n) for i in range(n)],
        ).astype(jnp.float32)
    return total.astype(jnp.bfloat16)


def body(inputs, gate_logits, kernel, cotangent, block_one, block_two):
    tokens = inputs[0]
    kernel_wide = kernel.astype(jnp.float32)
    grad_scale = (lax.axis_size("dp") * tokens.shape[2]) ** (-0.5)
    f32 = jnp.float32
    n_seq = lax.axis_size("seq")

    first = jnp.einsum(
        "acb,abd->acd", block_one, tokens, preferred_element_type=f32
    ).astype(jnp.bfloat16)
    first_cols = cols_recv(held(cols_send(first)))

    opened = jax.nn.sigmoid(gate_logits[0].astype(f32))
    incoming = cotangent[0].astype(f32)
    grad_fourth = held((incoming * opened).astype(jnp.bfloat16))
    grad_third = jnp.einsum(
        "fch,fhd->fcd", block_one, grad_fourth, preferred_element_type=f32
    ).astype(jnp.bfloat16)
    grad_third_send, first_cols = held((cols_send(grad_third), first_cols))
    grad_third_cols = cols_recv(grad_third_send)

    second = held(
        jnp.einsum("cea,acd->ecd", block_two, first_cols, preferred_element_type=f32)
    )
    filtered = (kernel_wide * second).astype(jnp.bfloat16)
    third = jnp.einsum(
        "cef,ecd->fcd", block_two, filtered, preferred_element_type=f32
    ).astype(jnp.bfloat16)
    third_send, grad_third_cols = held((natural(rows_send(third)), grad_third_cols))
    third_arrived = rows_move(third_send)

    grad_filtered = held(
        jnp.einsum("cef,fcd->ecd", block_two, grad_third_cols, preferred_element_type=f32)
    )
    grad_second = (kernel_wide * grad_filtered).astype(jnp.bfloat16)
    grad_first = jnp.einsum(
        "cea,ecd->acd", block_two, grad_second, preferred_element_type=f32
    ).astype(jnp.bfloat16)

    grad_kernel = (grad_filtered * second).astype(jnp.bfloat16)
    grad_block_two = (
        (
            jnp.einsum("fcd,ecd->cef", grad_third_cols, filtered, preferred_element_type=f32)
            + jnp.einsum("ecd,acd->cea", grad_second, first_cols, preferred_element_type=f32)
        )
        * grad_scale
    ).astype(jnp.bfloat16)
    grad_kernel = lax.psum_scatter(grad_kernel, "dp", scatter_dimension=2, tiled=True)
    grad_block_two = lax.psum_scatter(grad_block_two, "dp", scatter_dimension=2, tiled=True)

    own = grad_first.shape[0] // n_seq
    cut = 3 * own // 4 if own % 4 == 0 else own // 2
    halves = ((0, cut), (cut, own)) if cut else ((0, own),)
    grad_first_split = rows_send(grad_first)
    pieces = [grad_first_split[:, lo:hi] for lo, hi in halves]
    pieces, third_arrived = held((pieces, third_arrived))
    third_rows = rows_order(third_arrived)

    fourth = jnp.einsum(
        "fch,fcd->fhd", block_one, third_rows, preferred_element_type=f32
    ).astype(jnp.bfloat16)
    fourth_wide = natural(fourth).astype(f32)
    output = (opened * fourth_wide).astype(jnp.bfloat16)
    grad_gate = (incoming * fourth_wide * opened * (1.0 - opened)).astype(jnp.bfloat16)
    outer_one = jnp.einsum(
        "fhd,fcd->fch", grad_fourth, third_rows, preferred_element_type=f32
    )

    def finish(lo, hi, grad_first_rows):
        grad_tokens = natural(
            jnp.einsum(
                "acb,acd->abd", block_one[lo:hi], grad_first_rows, preferred_element_type=f32
            ).astype(jnp.bfloat16)
        )
        outer_inputs = jnp.einsum(
            "acd,abd->acb", grad_first_rows, tokens[lo:hi], preferred_element_type=f32
        )
        partial = (outer_one[lo:hi] + outer_inputs) * grad_scale
        return grad_tokens, dp_reduce_scatter(partial, 2)

    grad_tokens_parts, grad_block_ones = [], []
    pending = None
    for (lo, hi), piece in zip(halves, pieces):
        if pending is not None:
            piece, arrived, (output, grad_gate, outer_one) = held(
                (piece, pending[2], (output, grad_gate, outer_one))
            )
            done = finish(pending[0], pending[1], rows_order(arrived))
            grad_tokens_parts.append(done[0])
            grad_block_ones.append(done[1])
        pending = (lo, hi, rows_move(piece))
    arrived, grad_tokens_parts, output, grad_gate = held(
        (pending[2], grad_tokens_parts, output, grad_gate)
    )
    done = finish(pending[0], pending[1], rows_order(arrived))
    grad_tokens_parts.append(done[0])
    grad_block_ones.append(done[1])
    grad_tokens = jnp.concatenate(grad_tokens_parts, axis=0)
    grad_block_one = jnp.concatenate(grad_block_ones, axis=0)
    return (
        output[None],
        grad_tokens[None],
        grad_gate[None],
        grad_kernel,
        grad_block_one,
        grad_block_two,
    )


def solution(mesh):
    return jax.shard_map(
        body,
        mesh=mesh,
        in_specs=(
            P("dp", "seq", None, None),
            P("dp", "seq", None, None),
            P(None, "seq", None),
            P("dp", "seq", None, None),
            P("seq", None, None),
            P("seq", None, None),
        ),
        out_specs=(
            P("dp", "seq", None, None),
            P("dp", "seq", None, None),
            P("dp", "seq", None, None),
            P(None, "seq", "dp"),
            P("seq", None, "dp"),
            P("seq", None, "dp"),
        ),
        check_vma=False,
    )
```

```python
import jax
import jax.numpy as jnp
from jax import lax
from jax.sharding import PartitionSpec as P
from jax.experimental.layout import Layout, with_layout_constraint


def natural(x):
    return with_layout_constraint(x, Layout(tuple(range(x.ndim))))


def cols_send(x):
    n = lax.axis_size("seq")
    a, c, d = x.shape
    return x.reshape(a, n, c // n, d).transpose(1, 0, 2, 3)


def cols_recv(x):
    return lax.all_to_all(x, "seq", split_axis=0, concat_axis=0, tiled=True).reshape(
        (-1,) + x.shape[2:]
    )


def to_cols(x):
    return cols_recv(cols_send(x))


def rows_send(x):
    n = lax.axis_size("seq")
    return x.reshape((n, x.shape[0] // n) + x.shape[1:])


def rows_move(x):
    return lax.all_to_all(x, "seq", split_axis=0, concat_axis=0, tiled=True)


def rows_order(x):
    n, f, c, d = x.shape
    return x.transpose(1, 0, 2, 3).reshape(f, n * c, d)


def held(x):
    return lax.optimization_barrier(x)


def dp_reduce_scatter(x, dim):
    n = lax.axis_size("dp")
    me = lax.axis_index("dp")
    size = x.shape[dim] // n
    total = lax.dynamic_slice_in_dim(x, me * size, size, axis=dim)
    for shift in range(1, n):
        target = lax.rem(me + shift, n)
        part = lax.dynamic_slice_in_dim(x, target * size, size, axis=dim)
        total = total + lax.ppermute(
            part.astype(jnp.bfloat16),
            "dp",
            [(i, (i + shift) % n) for i in range(n)],
        ).astype(jnp.float32)
    return total.astype(jnp.bfloat16)


def body(inputs, gate_logits, kernel, cotangent, block_one, block_two):
    tokens = inputs[0]
    kernel_wide = kernel.astype(jnp.float32)
    grad_scale = (lax.axis_size("dp") * tokens.shape[2]) ** (-0.5)
    f32 = jnp.float32
    n_seq = lax.axis_size("seq")

    first = jnp.einsum(
        "acb,abd->acd", block_one, tokens, preferred_element_type=f32
    ).astype(jnp.bfloat16)
    first_cols = cols_recv(held(cols_send(first)))

    opened = jax.nn.sigmoid(gate_logits[0].astype(f32))
    incoming = cotangent[0].astype(f32)
    grad_fourth = held((incoming * opened).astype(jnp.bfloat16))
    grad_third = jnp.einsum(
        "fch,fhd->fcd", block_one, grad_fourth, preferred_element_type=f32
    ).astype(jnp.bfloat16)
    grad_third_send, first_cols = held((cols_send(grad_third), first_cols))
    grad_third_cols = cols_recv(grad_third_send)

    second = held(
        jnp.einsum("cea,acd->ecd", block_two, first_cols, preferred_element_type=f32)
    )
    filtered = (kernel_wide * second).astype(jnp.bfloat16)
    third = jnp.einsum(
        "cef,ecd->fcd", block_two, filtered, preferred_element_type=f32
    ).astype(jnp.bfloat16)
    third_send, grad_third_cols = held((natural(rows_send(third)), grad_third_cols))
    third_arrived = rows_move(third_send)

    grad_filtered = held(
        jnp.einsum("cef,fcd->ecd", block_two, grad_third_cols, preferred_element_type=f32)
    )
    grad_second = (kernel_wide * grad_filtered).astype(jnp.bfloat16)
    grad_first = jnp.einsum(
        "cea,ecd->acd", block_two, grad_second, preferred_element_type=f32
    ).astype(jnp.bfloat16)

    grad_kernel = (grad_filtered * second).astype(jnp.bfloat16)
    grad_block_two = (
        (
            jnp.einsum("fcd,ecd->cef", grad_third_cols, filtered, preferred_element_type=f32)
            + jnp.einsum("ecd,acd->cea", grad_second, first_cols, preferred_element_type=f32)
        )
        * grad_scale
    ).astype(jnp.bfloat16)
    grad_kernel = lax.psum_scatter(grad_kernel, "dp", scatter_dimension=2, tiled=True)
    grad_block_two = lax.psum_scatter(grad_block_two, "dp", scatter_dimension=2, tiled=True)

    own = grad_first.shape[0] // n_seq
    half = own // 2
    halves = ((0, half), (half, own)) if half else ((0, own),)
    grad_first_split = rows_send(grad_first)
    pieces = [grad_first_split[:, lo:hi] for lo, hi in halves]
    pieces, third_arrived = held((pieces, third_arrived))
    third_rows = rows_order(third_arrived)

    fourth = jnp.einsum(
        "fch,fcd->fhd", block_one, third_rows, preferred_element_type=f32
    ).astype(jnp.bfloat16)
    fourth_wide = natural(fourth).astype(f32)
    output = (opened * fourth_wide).astype(jnp.bfloat16)
    grad_gate = (incoming * fourth_wide * opened * (1.0 - opened)).astype(jnp.bfloat16)
    outer_one = jnp.einsum(
        "fhd,fcd->fch", grad_fourth, third_rows, preferred_element_type=f32
    )

    def finish(lo, hi, grad_first_rows):
        grad_tokens = natural(
            jnp.einsum(
                "acb,acd->abd", block_one[lo:hi], grad_first_rows, preferred_element_type=f32
            ).astype(jnp.bfloat16)
        )
        n_dp = lax.axis_size("dp")
        me = lax.axis_index("dp")
        size = tokens.shape[1] // n_dp

        def partial_for(owner):
            columns = lax.dynamic_slice_in_dim(tokens[lo:hi], owner * size, size, axis=1)
            known = lax.dynamic_slice_in_dim(outer_one[lo:hi], owner * size, size, axis=2)
            return (
                known
                + jnp.einsum(
                    "acd,abd->acb", grad_first_rows, columns, preferred_element_type=f32
                )
            ) * grad_scale

        received = []
        for shift in range(1, n_dp):
            target = lax.rem(me + shift, n_dp)
            received.append(
                lax.ppermute(
                    partial_for(target).astype(jnp.bfloat16),
                    "dp",
                    [(i, (i + shift) % n_dp) for i in range(n_dp)],
                )
            )
        total = partial_for(me)
        for part in received:
            total = total + part.astype(f32)
        return grad_tokens, total.astype(jnp.bfloat16)

    grad_tokens_parts, grad_block_ones = [], []
    pending = None
    for (lo, hi), piece in zip(halves, pieces):
        if pending is not None:
            piece, arrived, (output, grad_gate, outer_one) = held(
                (piece, pending[2], (output, grad_gate, outer_one))
            )
            done = finish(pending[0], pending[1], rows_order(arrived))
            grad_tokens_parts.append(done[0])
            grad_block_ones.append(done[1])
        pending = (lo, hi, rows_move(piece))
    arrived, grad_tokens_parts, output, grad_gate = held(
        (pending[2], grad_tokens_parts, output, grad_gate)
    )
    done = finish(pending[0], pending[1], rows_order(arrived))
    grad_tokens_parts.append(done[0])
    grad_block_ones.append(done[1])
    grad_tokens = jnp.concatenate(grad_tokens_parts, axis=0)
    grad_block_one = jnp.concatenate(grad_block_ones, axis=0)
    return (
        output[None],
        grad_tokens[None],
        grad_gate[None],
        grad_kernel,
        grad_block_one,
        grad_block_two,
    )


def solution(mesh):
    return jax.shard_map(
        body,
        mesh=mesh,
        in_specs=(
            P("dp", "seq", None, None),
            P("dp", "seq", None, None),
            P(None, "seq", None),
            P("dp", "seq", None, None),
            P("seq", None, None),
            P("seq", None, None),
        ),
        out_specs=(
            P("dp", "seq", None, None),
            P("dp", "seq", None, None),
            P("dp", "seq", None, None),
            P(None, "seq", "dp"),
            P("seq", None, "dp"),
            P("seq", None, "dp"),
        ),
        check_vma=False,
    )
```
